32 devices in a mesh: tm: 8 (over y, x, core), space: 4 (over z).
Axes of the slice: x: 2, y: 2, z: 4, core: 2. Of those that a mesh axis runs over, the one named last changes fastest.
Arguments:
- queries: bfloat16 [8, 4, 128, 1024], P('tm', 'space'), may hold values from -30 to 30
- key_vectors: bfloat16 [8, 4, 128, 1024], P('tm', 'space'), may hold values from -30 to 30
- value_vectors: bfloat16 [8, 4, 128, 1024], P('tm', 'space'), may hold values from -6 to 6
- key_blocks: int32 [8, 4, 2, 32], P('tm', 'space'), may hold values from 0 to 63, as said below
- block_count: int32 [8, 4, 2], P('tm', 'space'), may hold values from 1 to 32, as said below
Outputs:
- attention_out: bfloat16 [8, 4, 128, 1024], P('tm', 'space')
The draws below stay inside these ranges and needn't reach their ends.
Inputs may be any that keep to these rules, and one draw needn't show every extreme that they name: `key_blocks`: A row's entries are distinct ids of blocks in the query block's own band or an adjacent one, of any frame group; its first entry is the query block itself. Only the first block_count entries of a list are used; on some devices a list uses all 32.
All inputs are finite; a program needn't handle non-finite values.
Results may differ from the reference program's by a relative error of at most 0.0044.
Values may be sent and summed in bfloat16 or wider, within the bound.
No kernel may reach another device: no remote copies, remote signals or barrier semaphores. Data moves between devices by JAX's collectives and lax.ppermute only.
A program may use at most 128 MiB of HBM per device.

```python
import jax
import jax.numpy as jnp
from jax import lax

HEADS = 8
HDIM = 128
BLOCK = 64
PICKS = 32
TOK = 128
GROUPS = 8
BANDS = 4
QBLOCKS = 2


def pair_draw(key):
    base = jax.random.fold_in(key, 7)
    first, second = jax.random.split(base, 2)
    full_shape = (GROUPS, BANDS, TOK, HEADS * HDIM)
    query_part = jnp.clip(jax.random.normal(first, full_shape, jnp.float32), -6.0, 6.0)
    key_part = jnp.clip(jax.random.normal(second, full_shape, jnp.float32), -6.0, 6.0)
    return (query_part, key_part)


def draw_queries(key, part):
    return pair_draw(key)[0].astype(jnp.bfloat16)


def draw_key_vectors(key, part):
    return pair_draw(key)[1].astype(jnp.bfloat16)


def draw_key_blocks(key, part):
    per_band = GROUPS * QBLOCKS
    ncand = 3 * per_band
    candidate = jnp.arange(ncand, dtype=jnp.int32)
    offset = candidate // per_band - 1
    remainder = candidate % per_band
    group_of = remainder // QBLOCKS
    within = remainder % QBLOCKS
    group_idx = jnp.arange(GROUPS, dtype=jnp.int32)[:, None, None, None]
    band_idx = jnp.arange(BANDS, dtype=jnp.int32)[None, :, None, None]
    block_idx = jnp.arange(QBLOCKS, dtype=jnp.int32)[None, None, :, None]
    band_here = band_idx + offset[None, None, None, :]
    inside = (band_here >= 0) & (band_here < BANDS)
    itself = (offset[None, None, None, :] == 0) & (group_of[None, None, None, :] == group_idx) & (within[None, None, None, :] == block_idx)
    raw_draw = jax.random.randint(key, (GROUPS, BANDS, QBLOCKS, ncand), 0, 1 << 19, dtype=jnp.int32)
    scores = raw_draw * ncand + candidate
    scores = jnp.where(inside, scores, scores + (1 << 19) * ncand)
    scores = jnp.where(itself, -1, scores)
    picked = jnp.argsort(scores, axis=-1, stable=True)[..., :PICKS].astype(jnp.int32)
    picked_band = band_idx + picked // per_band - 1
    picked_rest = picked % per_band
    result = (picked_rest // QBLOCKS * BANDS + picked_band) * QBLOCKS + picked_rest % QBLOCKS
    return result.astype(jnp.int32)


def draw_block_count(key, part):
    first, second = jax.random.split(jax.random.fold_in(key, 11))
    shift_by = jax.random.randint(first, (), 0, 4, dtype=jnp.int32)
    group_idx = jnp.arange(GROUPS, dtype=jnp.int32)[:, None, None]
    band_idx = jnp.arange(BANDS, dtype=jnp.int32)[None, :, None]
    levels = 1 + (group_idx + band_idx + shift_by) % 4
    ceiling = jnp.maximum(PICKS * levels // 4, 1)
    raw_draw = jax.random.randint(second, (GROUPS, BANDS, QBLOCKS), 0, 1 << 20, dtype=jnp.int32)
    counts = raw_draw % ceiling + 1
    first_slot = jnp.arange(QBLOCKS, dtype=jnp.int32)[None, None, :] == 0
    counts = jnp.where(first_slot & (levels == 4), PICKS, counts)
    return counts.astype(jnp.int32)


def shard_levels(rng, shape, shards, smallest, high):
    level, own = 1.0, jax.random.fold_in(rng, 6)
    for axis_at, blocks in shards:
        draws = jnp.exp(jax.random.uniform(jax.random.fold_in(own, axis_at), (blocks,), jnp.float32, smallest / len(shards), high / len(shards)))
        level = level * jnp.repeat(draws, shape[axis_at] // blocks).reshape([-1 if axis == axis_at else 1 for axis in range(len(shape))])
    return level


def noise(stream_key, extent, scale, reach, cuts=(), kind=jnp.bfloat16):
    values = jax.random.normal(stream_key, extent, jnp.float32) * scale
    if len(cuts) > 0:
        values = shard_levels(stream_key, extent, cuts, -0.22, 0.18) * values
    return jnp.clip(values, min=-reach, max=reach).astype(kind)


def setup_inputs(seed: int = 0) -> dict:
    arg_keys = jax.random.split(jax.random.key(seed), 6)
    return {
        "queries": draw_queries(jax.random.fold_in(arg_keys[5], 71), 0),
        "key_vectors": draw_key_vectors(jax.random.fold_in(arg_keys[5], 71), 0),
        "value_vectors": noise(arg_keys[2], (GROUPS, BANDS, TOK, HEADS * HDIM), 1.0, 6.0, ((0, 8), (1, 4))),
        "key_blocks": draw_key_blocks(jax.random.fold_in(arg_keys[5], 71), 0),
        "block_count": draw_block_count(jax.random.fold_in(arg_keys[5], 71), 0),
    }


def reference(queries, key_vectors, value_vectors, key_blocks, block_count):
    feature_width = queries.shape[-1]
    query_tiles = queries.reshape(-1, BLOCK, feature_width)
    key_tiles = key_vectors.reshape(-1, BLOCK, feature_width)
    value_tiles = value_vectors.reshape(-1, BLOCK, feature_width)
    listed_all = key_blocks.reshape(-1, PICKS).astype(jnp.int32)
    counts_all = block_count.reshape(-1).astype(jnp.int32)

    def attend(packed):
        query_block, listed, count_here = packed
        key_rows = key_tiles[listed].reshape(PICKS * BLOCK, HEADS, HDIM).astype(jnp.float32)
        value_rows = value_tiles[listed].reshape(PICKS * BLOCK, HEADS, HDIM).astype(jnp.float32)
        query_rows = query_block.reshape(BLOCK, HEADS, HDIM).astype(jnp.float32)
        scores = jnp.einsum("qhd,khd->hqk", query_rows, key_rows) * (HDIM ** -0.5)
        usable = (jnp.arange(PICKS * BLOCK) // BLOCK) < count_here
        scores = jnp.where(usable[None, None, :], scores, -1e30)
        peaks = jnp.max(scores, axis=-1, keepdims=True)
        weights = jnp.exp(scores - peaks)
        totals = jnp.sum(weights, axis=-1)
        rounded = lax.optimization_barrier(weights.astype(jnp.bfloat16)).astype(jnp.float32)
        blended = jnp.einsum("hqk,khd->qhd", rounded, value_rows)
        result = blended / jnp.transpose(totals)[:, :, None]
        return result.reshape(BLOCK, feature_width).astype(jnp.bfloat16)

    outputs = lax.map(attend, (query_tiles, listed_all, counts_all))
    return outputs.reshape(queries.shape)
```

```python
import functools

import jax
import jax.numpy as jnp
from jax import lax
from jax.experimental import pallas as pl
from jax.experimental.pallas import tpu as pltpu
from jax.sharding import PartitionSpec as P

HEADS = 8
HDIM = 128
BLOCK = 64
PICKS = 32


def with_halo(cells, sides, width):
    for axis, dim in sides:
        count = lax.axis_size(axis)
        ends = count - 1
        head = lax.slice_in_dim(cells, 0, width, axis=dim)
        tail = lax.slice_in_dim(cells, cells.shape[dim] - width, cells.shape[dim], axis=dim)
        cells = jnp.concatenate(
            [
                lax.ppermute(tail, axis, [(i, (i + 1) % count) for i in range(ends)]),
                cells,
                lax.ppermute(head, axis, [((i + 1) % count, i) for i in range(ends)]),
            ],
            axis=dim,
        )
    return cells


def attend_kernel(slots_ref, counts_ref, q_ref, kv_hbm, o_ref, kbuf, vbuf, sems, *, blocks_here, tiles):
    feature_width = q_ref.shape[1]

    def copies(qb, p):
        slot = slots_ref[qb * PICKS + p]
        rows = pl.ds(pl.multiple_of(p * BLOCK, BLOCK), BLOCK)
        k_copy = pltpu.make_async_copy(kv_hbm.at[slot], kbuf.at[qb, rows], sems.at[0, qb, p])
        v_copy = pltpu.make_async_copy(kv_hbm.at[tiles + slot], vbuf.at[qb, rows], sems.at[1, qb, p])
        return k_copy, v_copy

    for qb in range(blocks_here):
        count = counts_ref[qb]

        def start(p, carry, qb=qb):
            for c in copies(qb, p):
                c.start()
            return carry

        def clear(p, carry, qb=qb):
            rows = pl.ds(pl.multiple_of(p * BLOCK, BLOCK), BLOCK)
            vbuf[qb, rows, :] = jnp.zeros((BLOCK, feature_width), vbuf.dtype)
            return carry

        lax.fori_loop(0, count, start, 0)
        lax.fori_loop(count, PICKS, clear, 0)

    for qb in range(blocks_here):
        count = counts_ref[qb]

        def finish(p, carry, qb=qb):
            for c in copies(qb, p):
                c.wait()
            return carry

        lax.fori_loop(0, count, finish, 0)
        column = lax.broadcasted_iota(jnp.int32, (BLOCK, PICKS * BLOCK), 1)
        usable = column < count * BLOCK
        for h in range(HEADS):
            cols = slice(h * HDIM, (h + 1) * HDIM)
            q_h = q_ref[qb * BLOCK:(qb + 1) * BLOCK, cols]
            k_h = kbuf[qb, :, cols]
            v_h = vbuf[qb, :, cols]
            scores = lax.dot_general(
                q_h, k_h, (((1,), (1,)), ((), ())), preferred_element_type=jnp.float32
            ) * HDIM ** (-0.5)
            scores = jnp.where(usable, scores, -1e30)
            peaks = jnp.max(scores, axis=-1, keepdims=True)
            weights = jnp.exp(scores - peaks)
            totals = jnp.sum(weights, axis=-1, keepdims=True)
            rounded = weights.astype(jnp.bfloat16)
            blended = jnp.dot(rounded, v_h, preferred_element_type=jnp.float32)
            o_ref[qb * BLOCK:(qb + 1) * BLOCK, cols] = (blended / totals).astype(o_ref.dtype)


def attend(query_rows, tile_set, slots, counts):
    tokens_here, feature_width = query_rows.shape
    blocks_here = tokens_here // BLOCK
    tiles = tile_set.shape[0] // 2
    kernel = functools.partial(attend_kernel, blocks_here=blocks_here, tiles=tiles)
    grid_spec = pltpu.PrefetchScalarGridSpec(
        num_scalar_prefetch=2,
        grid=(1,),
        in_specs=[
            pl.BlockSpec((tokens_here, feature_width), lambda i, s, c: (0, 0)),
            pl.BlockSpec(memory_space=pl.ANY),
        ],
        out_specs=pl.BlockSpec((tokens_here, feature_width), lambda i, s, c: (0, 0)),
        scratch_shapes=[
            pltpu.VMEM((blocks_here, PICKS * BLOCK, feature_width), tile_set.dtype),
            pltpu.VMEM((blocks_here, PICKS * BLOCK, feature_width), tile_set.dtype),
            pltpu.SemaphoreType.DMA((2, blocks_here, PICKS)),
        ],
    )
    return pl.pallas_call(
        kernel,
        grid_spec=grid_spec,
        out_shape=jax.ShapeDtypeStruct((tokens_here, feature_width), query_rows.dtype),
        compiler_params=pltpu.CompilerParams(vmem_limit_bytes=48 * 1024 * 1024),
    )(slots, counts, query_rows, tile_set)


def on_device(queries, key_vectors, value_vectors, key_blocks, block_count):
    tokens_here = queries.shape[2]
    feature_width = queries.shape[3]
    blocks_here = tokens_here // BLOCK
    stacked = jnp.stack([key_vectors, value_vectors])
    banded = with_halo(stacked, (("space", 2),), 1)
    gathered = lax.all_gather(banded, "tm", axis=1, tiled=True)
    groups = gathered.shape[1]
    tiles = groups * 3 * blocks_here
    tile_set = gathered.reshape(2 * tiles, BLOCK, feature_width)
    band_count = lax.axis_size("space")
    own_band = lax.axis_index("space")
    listed = key_blocks.reshape(blocks_here, PICKS)
    within = listed % blocks_here
    band_of = listed // blocks_here % band_count
    group_of = listed // (blocks_here * band_count)
    slots = (group_of * 3 + band_of - own_band + 1) * blocks_here + within
    slots = jnp.clip(slots, 0, tiles - 1).reshape(-1).astype(jnp.int32)
    counts = jnp.clip(block_count.reshape(blocks_here), 1, PICKS).astype(jnp.int32)
    result = attend(queries.reshape(tokens_here, feature_width), tile_set, slots, counts)
    return result.reshape(queries.shape)


def solution(mesh):
    in_specs = (
        P("tm", "space", None, None),
        P("tm", "space", None, None),
        P("tm", "space", None, None),
        P("tm", "space", None, None),
        P("tm", "space", None),
    )
    out_specs = P("tm", "space", None, None)
    return jax.shard_map(
        on_device, mesh=mesh, in_specs=in_specs, out_specs=out_specs, check_vma=False
    )
```

```python
import functools

import jax
import jax.numpy as jnp
from jax import lax
from jax.experimental import pallas as pl
from jax.experimental.pallas import tpu as pltpu
from jax.sharding import PartitionSpec as P

HEADS = 8
HDIM = 128
BLOCK = 64
PICKS = 32


def with_halo(cells, sides, width):
    for axis, dim in sides:
        count = lax.axis_size(axis)
        ends = count - 1
        head = lax.slice_in_dim(cells, 0, width, axis=dim)
        tail = lax.slice_in_dim(cells, cells.shape[dim] - width, cells.shape[dim], axis=dim)
        cells = jnp.concatenate(
            [
                lax.ppermute(tail, axis, [(i, (i + 1) % count) for i in range(ends)]),
                cells,
                lax.ppermute(head, axis, [((i + 1) % count, i) for i in range(ends)]),
            ],
            axis=dim,
        )
    return cells


def attend_kernel(where_ref, counts_ref, q_ref, *rest, blocks_here, pieces):
    sources = rest[:pieces]
    o_ref, kbuf, vbuf, sems = rest[pieces:]
    feature_width = q_ref.shape[1]
    bands_held = sources[0].shape[0] // 2

    def copies(qb, p, source):
        at = 2 * (qb * PICKS + p)
        row = where_ref[at + 1]
        rows = pl.ds(pl.multiple_of(p * BLOCK, BLOCK), BLOCK)
        k_copy = pltpu.make_async_copy(source.at[row], kbuf.at[qb, rows], sems.at[0, qb, p])
        v_copy = pltpu.make_async_copy(source.at[bands_held + row], vbuf.at[qb, rows], sems.at[1, qb, p])
        return k_copy, v_copy

    for qb in range(blocks_here):
        count = counts_ref[qb]

        def start(p, carry, qb=qb):
            piece = where_ref[2 * (qb * PICKS + p)]
            for j in range(pieces):
                @pl.when(piece == j)
                def _(j=j):
                    for c in copies(qb, p, sources[j]):
                        c.start()
            return carry

        def clear(p, carry, qb=qb):
            rows = pl.ds(pl.multiple_of(p * BLOCK, BLOCK), BLOCK)
            vbuf[qb, rows, :] = jnp.zeros((BLOCK, feature_width), vbuf.dtype)
            return carry

        lax.fori_loop(0, count, start, 0)
        lax.fori_loop(count, PICKS, clear, 0)

    for qb in range(blocks_here):
        count = counts_ref[qb]

        def finish(p, carry, qb=qb):
            for c in copies(qb, p, sources[0]):
                c.wait()
            return carry

        lax.fori_loop(0, count, finish, 0)
        column = lax.broadcasted_iota(jnp.int32, (BLOCK, PICKS * BLOCK), 1)
        usable = column < count * BLOCK
        for h in range(HEADS):
            cols = slice(h * HDIM, (h + 1) * HDIM)
            q_h = q_ref[qb * BLOCK:(qb + 1) * BLOCK, cols]
            k_h = kbuf[qb, :, cols]
            v_h = vbuf[qb, :, cols]
            scores = lax.dot_general(
                q_h, k_h, (((1,), (1,)), ((), ())), preferred_element_type=jnp.float32
            ) * HDIM ** (-0.5)
            scores = jnp.where(usable, scores, -1e30)
            peaks = jnp.max(scores, axis=-1, keepdims=True)
            weights = jnp.exp(scores - peaks)
            totals = jnp.sum(weights, axis=-1, keepdims=True)
            rounded = weights.astype(jnp.bfloat16)
            blended = jnp.dot(rounded, v_h, preferred_element_type=jnp.float32)
            o_ref[qb * BLOCK:(qb + 1) * BLOCK, cols] = (blended / totals).astype(o_ref.dtype)


def attend(query_rows, sources, where, counts):
    tokens_here, feature_width = query_rows.shape
    blocks_here = tokens_here // BLOCK
    kernel = functools.partial(attend_kernel, blocks_here=blocks_here, pieces=len(sources))
    grid_spec = pltpu.PrefetchScalarGridSpec(
        num_scalar_prefetch=2,
        grid=(1,),
        in_specs=[pl.BlockSpec((tokens_here, feature_width), lambda i, w, c: (0, 0))]
        + [pl.BlockSpec(memory_space=pl.ANY) for _ in sources],
        out_specs=pl.BlockSpec((tokens_here, feature_width), lambda i, w, c: (0, 0)),
        scratch_shapes=[
            pltpu.VMEM((blocks_here, PICKS * BLOCK, feature_width), query_rows.dtype),
            pltpu.VMEM((blocks_here, PICKS * BLOCK, feature_width), query_rows.dtype),
            pltpu.SemaphoreType.DMA((2, blocks_here, PICKS)),
        ],
    )
    return pl.pallas_call(
        kernel,
        grid_spec=grid_spec,
        out_shape=jax.ShapeDtypeStruct((tokens_here, feature_width), query_rows.dtype),
        compiler_params=pltpu.CompilerParams(vmem_limit_bytes=48 * 1024 * 1024),
    )(where, counts, query_rows, *sources)


def swap(piece, mask):
    count = lax.axis_size("tm")
    return lax.ppermute(piece, "tm", [(i, i ^ mask) for i in range(count)])


def on_device(queries, key_vectors, value_vectors, key_blocks, block_count):
    groups_here = queries.shape[0]
    tokens_here = queries.shape[2]
    feature_width = queries.shape[3]
    blocks_here = tokens_here // BLOCK
    members = lax.axis_size("tm")
    assert members & (members - 1) == 0 and members % 2 == 0
    stacked = jnp.stack([key_vectors, value_vectors])
    banded = with_halo(stacked, (("space", 2),), 1)
    tiles_per_piece = 2 * groups_here * 3 * blocks_here
    own = banded.reshape(tiles_per_piece, BLOCK, feature_width)
    pieces = [own] * members
    for mask in range(2, members, 2):
        pieces[mask] = swap(own, mask)
    for mask in range(0, members, 2):
        pieces[mask + 1] = swap(pieces[mask], 1)
    band_count = lax.axis_size("space")
    own_band = lax.axis_index("space")
    me = lax.axis_index("tm")
    listed = key_blocks.reshape(blocks_here, PICKS)
    within = listed % blocks_here
    band_of = listed // blocks_here % band_count
    group_of = listed // (blocks_here * band_count)
    holder = jnp.clip(group_of // groups_here, 0, members - 1)
    piece = jnp.bitwise_xor(holder, me)
    row = ((group_of % groups_here) * 3 + band_of - own_band + 1) * blocks_here + within
    row = jnp.clip(row, 0, tiles_per_piece // 2 - 1)
    where = jnp.stack([piece, row], axis=-1).reshape(-1).astype(jnp.int32)
    counts = jnp.clip(block_count.reshape(blocks_here), 1, PICKS).astype(jnp.int32)
    result = attend(queries.reshape(tokens_here, feature_width), pieces, where, counts)
    return result.reshape(queries.shape)


def solution(mesh):
    in_specs = (
        P("tm", "space", None, None),
        P("tm", "space", None, None),
        P("tm", "space", None, None),
        P("tm", "space", None, None),
        P("tm", "space", None),
    )
    out_specs = P("tm", "space", None, None)
    return jax.shard_map(
        on_device, mesh=mesh, in_specs=in_specs, out_specs=out_specs, check_vma=False
    )
```

```python
import functools

import jax
import jax.numpy as jnp
from jax import lax
from jax.experimental import pallas as pl
from jax.experimental.pallas import tpu as pltpu
from jax.sharding import PartitionSpec as P

HEADS = 8
HDIM = 128
BLOCK = 64
PICKS = 32


def with_halo(cells, sides, width):
    for axis, dim in sides:
        count = lax.axis_size(axis)
        ends = count - 1
        head = lax.slice_in_dim(cells, 0, width, axis=dim)
        tail = lax.slice_in_dim(cells, cells.shape[dim] - width, cells.shape[dim], axis=dim)
        cells = jnp.concatenate(
            [
                lax.ppermute(tail, axis, [(i, (i + 1) % count) for i in range(ends)]),
                cells,
                lax.ppermute(head, axis, [((i + 1) % count, i) for i in range(ends)]),
            ],
            axis=dim,
        )
    return cells


def attend_kernel(slots_ref, counts_ref, q_ref, kv_hbm, o_ref, kbuf, vbuf, sems, *, blocks_here, tiles):
    feature_width = q_ref.shape[1]

    def copies(qb, p):
        slot = slots_ref[qb * PICKS + p]
        rows = pl.ds(pl.multiple_of(p * BLOCK, BLOCK), BLOCK)
        k_copy = pltpu.make_async_copy(kv_hbm.at[slot], kbuf.at[qb, rows], sems.at[0, qb, p])
        v_copy = pltpu.make_async_copy(kv_hbm.at[tiles + slot], vbuf.at[qb, rows], sems.at[1, qb, p])
        return k_copy, v_copy

    for qb in range(blocks_here):
        count = counts_ref[qb]

        def start(p, carry, qb=qb):
            for c in copies(qb, p):
                c.start()
            return carry

        def clear(p, carry, qb=qb):
            rows = pl.ds(pl.multiple_of(p * BLOCK, BLOCK), BLOCK)
            vbuf[qb, rows, :] = jnp.zeros((BLOCK, feature_width), vbuf.dtype)
            return carry

        lax.fori_loop(0, count, start, 0)
        lax.fori_loop(count, PICKS, clear, 0)

    for qb in range(blocks_here):
        count = counts_ref[qb]

        def finish(p, carry, qb=qb):
            for c in copies(qb, p):
                c.wait()
            return carry

        lax.fori_loop(0, count, finish, 0)
        column = lax.broadcasted_iota(jnp.int32, (BLOCK, PICKS * BLOCK), 1)
        usable = column < count * BLOCK
        for h in range(HEADS):
            cols = slice(h * HDIM, (h + 1) * HDIM)
            q_h = q_ref[qb * BLOCK:(qb + 1) * BLOCK, cols]
            k_h = kbuf[qb, :, cols]
            v_h = vbuf[qb, :, cols]
            scores = lax.dot_general(
                q_h, k_h, (((1,), (1,)), ((), ())), preferred_element_type=jnp.float32
            ) * HDIM ** (-0.5)
            scores = jnp.where(usable, scores, -1e30)
            peaks = jnp.max(scores, axis=-1, keepdims=True)
            weights = jnp.exp(scores - peaks)
            totals = jnp.sum(weights, axis=-1, keepdims=True)
            rounded = weights.astype(jnp.bfloat16)
            blended = jnp.dot(rounded, v_h, preferred_element_type=jnp.float32)
            o_ref[qb * BLOCK:(qb + 1) * BLOCK, cols] = (blended / totals).astype(o_ref.dtype)


def attend(query_rows, tile_set, slots, counts):
    tokens_here, feature_width = query_rows.shape
    blocks_here = tokens_here // BLOCK
    tiles = tile_set.shape[0] // 2
    kernel = functools.partial(attend_kernel, blocks_here=blocks_here, tiles=tiles)
    grid_spec = pltpu.PrefetchScalarGridSpec(
        num_scalar_prefetch=2,
        grid=(1,),
        in_specs=[
            pl.BlockSpec((tokens_here, feature_width), lambda i, s, c: (0, 0)),
            pl.BlockSpec(memory_space=pl.ANY),
        ],
        out_specs=pl.BlockSpec((tokens_here, feature_width), lambda i, s, c: (0, 0)),
        scratch_shapes=[
            pltpu.VMEM((blocks_here, PICKS * BLOCK, feature_width), tile_set.dtype),
            pltpu.VMEM((blocks_here, PICKS * BLOCK, feature_width), tile_set.dtype),
            pltpu.SemaphoreType.DMA((2, blocks_here, PICKS)),
        ],
    )
    return pl.pallas_call(
        kernel,
        grid_spec=grid_spec,
        out_shape=jax.ShapeDtypeStruct((tokens_here, feature_width), query_rows.dtype),
        compiler_params=pltpu.CompilerParams(vmem_limit_bytes=48 * 1024 * 1024),
    )(slots, counts, query_rows, tile_set)


def on_device(queries, key_vectors, value_vectors, key_blocks, block_count):
    groups_here = queries.shape[0]
    tokens_here = queries.shape[2]
    feature_width = queries.shape[3]
    blocks_here = tokens_here // BLOCK
    chips = lax.axis_size("chip")
    cores = lax.axis_size("core")
    stacked = jnp.stack([key_vectors, value_vectors])
    banded = with_halo(stacked, (("space", 2),), 1)
    across = lax.all_gather(banded, "chip", axis=1, tiled=True)
    gathered = lax.all_gather(across, "core", axis=1, tiled=True)
    tiles = cores * chips * groups_here * 3 * blocks_here
    tile_set = gathered.reshape(2 * tiles, BLOCK, feature_width)
    band_count = lax.axis_size("space")
    own_band = lax.axis_index("space")
    listed = key_blocks.reshape(blocks_here, PICKS)
    within = listed % blocks_here
    band_of = listed // blocks_here % band_count
    group_of = listed // (blocks_here * band_count)
    holder = group_of // groups_here
    order = (holder % cores) * chips + holder // cores
    slots = ((order * groups_here + group_of % groups_here) * 3 + band_of - own_band + 1) * blocks_here + within
    slots = jnp.clip(slots, 0, tiles - 1).reshape(-1).astype(jnp.int32)
    counts = jnp.clip(block_count.reshape(blocks_here), 1, PICKS).astype(jnp.int32)
    result = attend(queries.reshape(tokens_here, feature_width), tile_set, slots, counts)
    return result.reshape(queries.shape)


def solution(mesh):
    members = mesh.shape["tm"]
    devices = mesh.devices.reshape(members // 2, 2, mesh.shape["space"])
    split = jax.sharding.Mesh(devices, ("chip", "core", "space"))
    rows = ("chip", "core")
    in_specs = (
        P(rows, "space", None, None),
        P(rows, "space", None, None),
        P(rows, "space", None, None),
        P(rows, "space", None, None),
        P(rows, "space", None),
    )
    out_specs = P(rows, "space", None, None)
    return jax.shard_map(
        on_device, mesh=split, in_specs=in_specs, out_specs=out_specs, check_vma=False
    )
```

```python
import functools

import jax
import jax.numpy as jnp
from jax import lax
from jax.experimental import pallas as pl
from jax.experimental.pallas import tpu as pltpu
from jax.sharding import PartitionSpec as P

HEADS = 8
HDIM = 128
BLOCK = 64
PICKS = 32


def dispatch(index, low, high, act):
    if high - low == 1:
        act(low)
        return
    middle = (low + high) // 2

    @pl.when(index < middle)
    def _():
        dispatch(index, low, middle, act)

    @pl.when(index >= middle)
    def _():
        dispatch(index, middle, high, act)


def attend_kernel(where_ref, counts_ref, q_ref, *rest, blocks_here, pieces):
    sources = rest[:pieces]
    o_ref, kvbuf, sems = rest[pieces:]
    feature_width = q_ref.shape[1]

    def copy(qb, p, source):
        row = where_ref[2 * (qb * PICKS + p) + 1]
        return pltpu.make_async_copy(source.at[row], kvbuf.at[qb, p], sems.at[qb, p])

    for qb in range(blocks_here):
        count = counts_ref[qb]

        def start(p, carry, qb=qb):
            piece = where_ref[2 * (qb * PICKS + p)]

            def act(j):
                copy(qb, p, sources[j]).start()

            dispatch(piece, 0, pieces, act)
            return carry

        def clear(p, carry, qb=qb):
            kvbuf[qb, p, 1] = jnp.zeros((BLOCK, feature_width), kvbuf.dtype)
            return carry

        lax.fori_loop(0, count, start, 0)
        lax.fori_loop(count, PICKS, clear, 0)

    for qb in range(blocks_here):
        count = counts_ref[qb]

        def finish(p, carry, qb=qb):
            copy(qb, p, sources[0]).wait()
            return carry

        lax.fori_loop(0, count, finish, 0)
        column = lax.broadcasted_iota(jnp.int32, (BLOCK, PICKS * BLOCK), 1)
        usable = column < count * BLOCK
        for h in range(HEADS):
            cols = slice(h * HDIM, (h + 1) * HDIM)
            q_h = q_ref[qb * BLOCK:(qb + 1) * BLOCK, cols]
            k_h = kvbuf[qb, :, 0, :, cols].reshape(PICKS * BLOCK, HDIM)
            v_h = kvbuf[qb, :, 1, :, cols].reshape(PICKS * BLOCK, HDIM)
            scores = lax.dot_general(
                q_h, k_h, (((1,), (1,)), ((), ())), preferred_element_type=jnp.float32
            ) * HDIM ** (-0.5)
            scores = jnp.where(usable, scores, -1e30)
            peaks = jnp.max(scores, axis=-1, keepdims=True)
            weights = jnp.exp(scores - peaks)
            totals = jnp.sum(weights, axis=-1, keepdims=True)
            rounded = weights.astype(jnp.bfloat16)
            blended = jnp.dot(rounded, v_h, preferred_element_type=jnp.float32)
            o_ref[qb * BLOCK:(qb + 1) * BLOCK, cols] = (blended / totals).astype(o_ref.dtype)


def attend(query_rows, sources, where, counts):
    tokens_here, feature_width = query_rows.shape
    blocks_here = tokens_here // BLOCK
    kernel = functools.partial(attend_kernel, blocks_here=blocks_here, pieces=len(sources))
    grid_spec = pltpu.PrefetchScalarGridSpec(
        num_scalar_prefetch=2,
        grid=(1,),
        in_specs=[pl.BlockSpec((tokens_here, feature_width), lambda i, w, c: (0, 0))]
        + [pl.BlockSpec(memory_space=pl.ANY) for _ in sources],
        out_specs=pl.BlockSpec((tokens_here, feature_width), lambda i, w, c: (0, 0)),
        scratch_shapes=[
            pltpu.VMEM((blocks_here, PICKS, 2, BLOCK, feature_width), query_rows.dtype),
            pltpu.SemaphoreType.DMA((blocks_here, PICKS)),
        ],
    )
    return pl.pallas_call(
        kernel,
        grid_spec=grid_spec,
        out_shape=jax.ShapeDtypeStruct((tokens_here, feature_width), query_rows.dtype),
        compiler_params=pltpu.CompilerParams(vmem_limit_bytes=48 * 1024 * 1024),
    )(where, counts, query_rows, *sources)


def swap(piece, mask):
    count = lax.axis_size("tm")
    return lax.ppermute(piece, "tm", [(i, i ^ mask) for i in range(count)])


def exchange(own, masks):
    pieces = {0: own}
    for mask in masks:
        if mask % 2 == 0 and mask > 0:
            pieces[mask] = swap(own, mask)
    for mask in masks:
        if mask % 2 == 1:
            pieces[mask] = swap(pieces[mask - 1], 1)
    return [pieces[mask] for mask in masks]


def on_device(queries, key_vectors, value_vectors, key_blocks, block_count):
    groups_here = queries.shape[0]
    tokens_here = queries.shape[2]
    feature_width = queries.shape[3]
    blocks_here = tokens_here // BLOCK
    members = lax.axis_size("tm")
    assert members & (members - 1) == 0 and members % 2 == 0
    far = members - 2
    split = (groups_here, 1, blocks_here, BLOCK, feature_width)
    stacked = jnp.stack([key_vectors.reshape(split), value_vectors.reshape(split)], axis=3)
    per_band = groups_here * blocks_here
    gathered = lax.all_gather(stacked, "tm", axis=0, tiled=True)
    gathered = gathered.reshape(members * per_band, 2, BLOCK, feature_width)
    me = lax.axis_index("tm")
    far_piece = lax.dynamic_slice_in_dim(gathered, jnp.bitwise_xor(me, far) * per_band, per_band, axis=0)
    count = lax.axis_size("space")
    ends = count - 1
    up = [(i, i + 1) for i in range(ends)]
    down = [(i + 1, i) for i in range(ends)]
    below = lax.ppermute(stacked, "space", up)
    above = lax.ppermute(stacked, "space", down)
    halo = jnp.concatenate([below, above], axis=1)
    sides = exchange(halo.reshape(2 * per_band, 2, BLOCK, feature_width), list(range(far)))
    from_below = lax.ppermute(far_piece, "space", up)
    from_above = lax.ppermute(far_piece, "space", down)
    relayed = [from_below, swap(from_below, 1), from_above, swap(from_above, 1)]
    own_band = lax.axis_index("space")
    listed = key_blocks.reshape(blocks_here, PICKS)
    within = listed % blocks_here
    band_of = listed // blocks_here % count
    group_of = jnp.clip(listed // (blocks_here * count), 0, members * groups_here - 1)
    holder = group_of // groups_here
    shift = band_of - own_band
    mask = jnp.bitwise_xor(holder, me)
    piece = jnp.where(shift == 0, 0, 1 + mask + jnp.where((mask >= far) & (shift > 0), 2, 0))
    local = group_of % groups_here
    side = jnp.where(shift < 0, 0, 1)
    row = jnp.where((shift == 0) | (mask >= far), local, local * 2 + side) * blocks_here + within
    row = jnp.where(shift == 0, holder * per_band + row, row)
    where = jnp.stack([piece, row], axis=-1).reshape(-1).astype(jnp.int32)
    counts = jnp.clip(block_count.reshape(blocks_here), 1, PICKS).astype(jnp.int32)
    sources = [gathered] + sides + relayed
    result = attend(queries.reshape(tokens_here, feature_width), sources, where, counts)
    return result.reshape(queries.shape)


def solution(mesh):
    in_specs = (
        P("tm", "space", None, None),
        P("tm", "space", None, None),
        P("tm", "space", None, None),
        P("tm", "space", None, None),
        P("tm", "space", None),
    )
    out_specs = P("tm", "space", None, None)
    return jax.shard_map(
        on_device, mesh=mesh, in_specs=in_specs, out_specs=out_specs, check_vma=False
    )
```

```python
import functools

import jax
import jax.numpy as jnp
from jax import lax
from jax.experimental import pallas as pl
from jax.experimental.pallas import tpu as pltpu
from jax.sharding import PartitionSpec as P

HEADS = 8
HDIM = 128
BLOCK = 64
PICKS = 32


def dispatch(index, low, high, act):
    if high - low == 1:
        act(low)
        return
    middle = (low + high) // 2

    @pl.when(index < middle)
    def _():
        dispatch(index, low, middle, act)

    @pl.when(index >= middle)
    def _():
        dispatch(index, middle, high, act)


def attend_kernel(where_ref, counts_ref, q_ref, *rest, blocks_here, pieces):
    sources = rest[:pieces]
    o_ref, kvbuf, sems = rest[pieces:]
    feature_width = q_ref.shape[1]

    def copy(qb, p, source):
        row = where_ref[2 * (qb * PICKS + p) + 1]
        return pltpu.make_async_copy(source.at[row], kvbuf.at[qb, p], sems.at[qb, p])

    for qb in range(blocks_here):
        count = counts_ref[qb]

        def start(p, carry, qb=qb):
            piece = where_ref[2 * (qb * PICKS + p)]

            def act(j):
                copy(qb, p, sources[j]).start()

            dispatch(piece, 0, pieces, act)
            return carry

        def clear(p, carry, qb=qb):
            kvbuf[qb, p, 1] = jnp.zeros((BLOCK, feature_width), kvbuf.dtype)
            return carry

        lax.fori_loop(0, count, start, 0)
        lax.fori_loop(count, PICKS, clear, 0)

    for qb in range(blocks_here):
        count = counts_ref[qb]

        def finish(p, carry, qb=qb):
            copy(qb, p, sources[0]).wait()
            return carry

        lax.fori_loop(0, count, finish, 0)
        column = lax.broadcasted_iota(jnp.int32, (BLOCK, PICKS * BLOCK), 1)
        usable = column < count * BLOCK
        for h in range(HEADS):
            cols = slice(h * HDIM, (h + 1) * HDIM)
            q_h = q_ref[qb * BLOCK:(qb + 1) * BLOCK, cols]
            k_h = kvbuf[qb, :, 0, :, cols].reshape(PICKS * BLOCK, HDIM)
            v_h = kvbuf[qb, :, 1, :, cols].reshape(PICKS * BLOCK, HDIM)
            scores = lax.dot_general(
                q_h, k_h, (((1,), (1,)), ((), ())), preferred_element_type=jnp.float32
            ) * HDIM ** (-0.5)
            scores = jnp.where(usable, scores, -1e30)
            peaks = jnp.max(scores, axis=-1, keepdims=True)
            weights = jnp.exp(scores - peaks)
            totals = jnp.sum(weights, axis=-1, keepdims=True)
            rounded = weights.astype(jnp.bfloat16)
            blended = jnp.dot(rounded, v_h, preferred_element_type=jnp.float32)
            o_ref[qb * BLOCK:(qb + 1) * BLOCK, cols] = (blended / totals).astype(o_ref.dtype)


def attend(query_rows, sources, where, counts):
    tokens_here, feature_width = query_rows.shape
    blocks_here = tokens_here // BLOCK
    kernel = functools.partial(attend_kernel, blocks_here=blocks_here, pieces=len(sources))
    grid_spec = pltpu.PrefetchScalarGridSpec(
        num_scalar_prefetch=2,
        grid=(1,),
        in_specs=[pl.BlockSpec((tokens_here, feature_width), lambda i, w, c: (0, 0))]
        + [pl.BlockSpec(memory_space=pl.ANY) for _ in sources],
        out_specs=pl.BlockSpec((tokens_here, feature_width), lambda i, w, c: (0, 0)),
        scratch_shapes=[
            pltpu.VMEM((blocks_here, PICKS, 2, BLOCK, feature_width), query_rows.dtype),
            pltpu.SemaphoreType.DMA((blocks_here, PICKS)),
        ],
    )
    return pl.pallas_call(
        kernel,
        grid_spec=grid_spec,
        out_shape=jax.ShapeDtypeStruct((tokens_here, feature_width), query_rows.dtype),
        compiler_params=pltpu.CompilerParams(vmem_limit_bytes=48 * 1024 * 1024),
    )(where, counts, query_rows, *sources)


def swap(piece, mask):
    count = lax.axis_size("tm")
    return lax.ppermute(piece, "tm", [(i, i ^ mask) for i in range(count)])


def exchange(own, masks):
    pieces = {0: own}
    for mask in masks:
        if mask % 2 == 0 and mask > 0:
            pieces[mask] = swap(own, mask)
    for mask in masks:
        if mask % 2 == 1:
            pieces[mask] = swap(pieces[mask - 1], 1)
    return [pieces[mask] for mask in masks]


def on_device(queries, key_vectors, value_vectors, key_blocks, block_count):
    groups_here = queries.shape[0]
    tokens_here = queries.shape[2]
    feature_width = queries.shape[3]
    blocks_here = tokens_here // BLOCK
    members = lax.axis_size("tm")
    assert members & (members - 1) == 0 and members % 2 == 0
    far = members - 2
    split = (groups_here, 1, blocks_here, BLOCK, feature_width)
    stacked = jnp.stack([key_vectors.reshape(split), value_vectors.reshape(split)], axis=3)
    per_band = groups_here * blocks_here
    tile = (per_band, 2, BLOCK, feature_width)
    middle = exchange(stacked.reshape(tile), list(range(members)))
    count = lax.axis_size("space")
    ends = count - 1
    toward = [[(i, i + 1) for i in range(ends)], [(i + 1, i) for i in range(ends)]]
    bands = [lax.ppermute(stacked, "space", toward[d]).reshape(tile) for d in range(2)]
    sources = list(middle)
    table = [[None, None] for _ in range(members)]
    for d in range(2):
        for mask, piece in enumerate([bands[d], swap(bands[d], 1)]):
            table[mask][d] = (len(sources), 0)
            sources.append(piece)
    for mask in range(2, members, 2):
        direct = [] if mask == far else [(mask // 2 + 1) % 2]
        for d in range(2):
            if d in direct:
                first = swap(bands[d], mask)
            else:
                first = lax.ppermute(middle[mask], "space", toward[d])
            for j, piece in enumerate([first, swap(first, 1)]):
                table[mask + j][d] = (len(sources), 0)
                sources.append(piece)
    lookup_piece = jnp.array([[table[m][d][0] for d in range(2)] for m in range(members)], jnp.int32)
    lookup_base = jnp.array([[table[m][d][1] for d in range(2)] for m in range(members)], jnp.int32)
    own_band = lax.axis_index("space")
    me = lax.axis_index("tm")
    listed = key_blocks.reshape(blocks_here, PICKS)
    within = listed % blocks_here
    band_of = listed // blocks_here % count
    group_of = jnp.clip(listed // (blocks_here * count), 0, members * groups_here - 1)
    holder = group_of // groups_here
    shift = band_of - own_band
    mask = jnp.bitwise_xor(holder, me)
    d = jnp.where(shift > 0, 1, 0)
    local = (group_of % groups_here) * blocks_here + within
    piece = jnp.where(shift == 0, mask, lookup_piece[mask, d])
    row = jnp.where(shift == 0, local, lookup_base[mask, d] + local)
    where = jnp.stack([piece, row], axis=-1).reshape(-1).astype(jnp.int32)
    counts = jnp.clip(block_count.reshape(blocks_here), 1, PICKS).astype(jnp.int32)
    result = attend(queries.reshape(tokens_here, feature_width), sources, where, counts)
    return result.reshape(queries.shape)


def solution(mesh):
    in_specs = (
        P("tm", "space", None, None),
        P("tm", "space", None, None),
        P("tm", "space", None, None),
        P("tm", "space", None, None),
        P("tm", "space", None),
    )
    out_specs = P("tm", "space", None, None)
    return jax.shard_map(
        on_device, mesh=mesh, in_specs=in_specs, out_specs=out_specs, check_vma=False
    )
```
